32 devices in a mesh: rows: 16 (over z, y, x), grp: 2 (over core).
Axes of the slice: x: 2, y: 2, z: 4, core: 2. Of those that a mesh axis runs over, the one named last changes fastest.
Arguments:
- slab_x: bfloat16 [131072, 512], P(('rows', 'grp'))
- slab_y: bfloat16 [131072, 256], P(('rows', 'grp')), may hold values from -6 to 6
- row_mask: int32 [131072], P(('rows', 'grp')), may hold values 0 or 1
- live_tiles: int32 [32], P(('rows', 'grp')), may hold values from 1 to 32, as said below
- old_r: float32 [512, 512], P('rows'), as said below
- old_z: float32 [512, 256], P('rows'), may hold values from -6 to 6
Outputs:
- new_r: float32 [512, 512], replicated
- new_z: float32 [512, 256], replicated
The draws below stay inside these ranges and needn't reach their ends.
Inputs may be any that keep to these rules, and one draw needn't show every extreme that they name: `live_tiles`: live tiles of each device; at least one device has all 32. old_r is upper triangular with diagonal entries from 0.5 to 2.
All inputs are finite; a program needn't handle non-finite values. No bound on the sum of `row_mask` on one device may be relied on, other than what follows from the above.
Results may differ from the reference program's by a relative error of at most 0.0003.
Values sent between devices are 32-bit elements; how exact they have to be, the bound alone decides.
No kernel may reach another device: no remote copies, remote signals or barrier semaphores. Data moves between devices by JAX's collectives and lax.ppermute only.
A program may use at most 64 MiB of HBM per device.

```python
import math
import jax
import jax.numpy as jnp
from jax import lax

P_SIZE = 512
RESP = 256
ROWS_DEV = 4096
TILE = 128
TILES_DEV = 32
ROWS = 131072
N_ROWS = 16
N_GRP = 2


def draw_slab_x(key, part):
    first, second, third = jax.random.split(key, 3)
    base = jax.random.normal(first, (ROWS, P_SIZE), jnp.float32)
    row_scale = jnp.exp(jax.random.uniform(second, (ROWS, 1), jnp.float32) * math.log(10.0))
    col_scale = jnp.exp(jax.random.uniform(third, (1, P_SIZE), jnp.float32, math.log(0.5), math.log(2.0)))
    return (base * row_scale * col_scale * (0.4 / math.sqrt(ROWS))).astype(jnp.bfloat16)


def draw_live_tiles(key, part):
    count = N_ROWS * N_GRP
    first, second = jax.random.split(jax.random.fold_in(key, 11))
    raw = jax.random.randint(first, (count,), 0, TILES_DEV + 1)
    tiles = jnp.maximum(1, raw * raw // TILES_DEV)
    pick = jax.random.randint(second, (), 0, count)
    return jnp.where(jnp.arange(count) == pick, TILES_DEV, tiles).astype(jnp.int32)


def draw_old_r(key, part):
    first, second = jax.random.split(jax.random.fold_in(key, 23))
    row_ids = jnp.arange(P_SIZE)[:, None]
    col_ids = jnp.arange(P_SIZE)[None, :]
    off = jax.random.normal(first, (P_SIZE, P_SIZE), jnp.float32)
    diag = jnp.exp(jax.random.uniform(second, (P_SIZE, 1), jnp.float32, math.log(0.5), math.log(2.0)))
    upper = jnp.where(col_ids > row_ids, off * (0.5 / math.sqrt(P_SIZE)), 0.0)
    return jnp.where(col_ids == row_ids, diag, upper).astype(jnp.float32)


def touch_ends(array, own_key, least, largest):
    longest = array.shape.index(max(array.shape))
    spots = []
    for shift in (0, 1):
        where = [jax.random.randint(jax.random.fold_in(own_key, axis), (), 0, length) for axis, length in enumerate(array.shape)]
        where[longest] = (where[longest] + shift) % array.shape[longest]
        spots.append(tuple(where))
    return array.at[spots[0]].set(least).at[spots[1]].set(largest)


def block_levels(stream_key, dims, cuts, low, high):
    def one(axis_at, blocks):
        steps = jax.random.uniform(jax.random.fold_in(jax.random.fold_in(stream_key, 6), axis_at), (blocks,), jnp.float32, low / len(cuts), high / len(cuts))
        return jnp.repeat(jnp.exp(steps), dims[axis_at] // blocks).reshape((-1,) + (1,) * (len(dims) - axis_at - 1))

    factor_of = one(*cuts[0])
    for cut in cuts[1:]:
        factor_of = factor_of * one(*cut)
    return factor_of


def noise(stream_key, extent, width, most, cuts=(), held_as=jnp.bfloat16):
    entries = width * jax.random.normal(stream_key, extent, jnp.float32)
    if cuts:
        entries = entries * block_levels(stream_key, extent, cuts, -0.22, 0.18)
    return jnp.clip(entries, -most, most).astype(held_as)


def setup_inputs(seed: int = 0) -> dict:
    key_list = jax.random.split(jax.random.key(seed), 7)
    slab_x = draw_slab_x(jax.random.fold_in(key_list[6], 71), 0)
    slab_y = noise(key_list[1], (ROWS, RESP), 1.0, 6.0, ((0, 32),))
    row_mask = touch_ends((jax.random.randint(key_list[2], (ROWS,), 0, 8) < 7).astype(jnp.int32), jax.random.fold_in(key_list[2], 1), 0, 1)
    live_tiles = draw_live_tiles(jax.random.fold_in(key_list[6], 71), 0)
    old_r = draw_old_r(jax.random.fold_in(key_list[6], 71), 0)
    old_z = noise(key_list[5], (P_SIZE, RESP), 1.0, 6.0, ((0, 16),), jnp.float32)
    return {"slab_x": slab_x, "slab_y": slab_y, "row_mask": row_mask, "live_tiles": live_tiles, "old_r": old_r, "old_z": old_z}


def reference(slab_x, slab_y, row_mask, live_tiles, old_r, old_z):
    devs = live_tiles.shape[0]
    xs = slab_x.reshape(devs, ROWS_DEV, P_SIZE)
    ys = slab_y.reshape(devs, ROWS_DEV, RESP)
    ms = row_mask.reshape(devs, ROWS_DEV)
    tile_ids = (jnp.arange(ROWS_DEV, dtype=jnp.int32) // TILE).astype(jnp.int32)

    def device_terms(totals, item):
        x_rows, y_rows, m_rows, count = item
        live = (m_rows == 1) & (tile_ids < count)
        masked = jnp.where(live[:, None], x_rows, jnp.zeros_like(x_rows))
        gram = jnp.dot(masked.T.astype(jnp.float32), x_rows.astype(jnp.float32), preferred_element_type=jnp.float32)
        cross = jnp.dot(masked.T.astype(jnp.float32), y_rows.astype(jnp.float32), preferred_element_type=jnp.float32)
        return ((totals[0] + gram, totals[1] + cross), None)
    init = (jnp.zeros((P_SIZE, P_SIZE), jnp.float32), jnp.zeros((P_SIZE, RESP), jnp.float32))
    (gram, cross), _ = lax.scan(device_terms, init, (xs, ys, ms, live_tiles))
    total = jnp.dot(old_r.T.astype(jnp.float32), old_r.astype(jnp.float32), precision=lax.Precision.HIGHEST, preferred_element_type=jnp.float32) + gram
    rhs = jnp.dot(old_r.T.astype(jnp.float32), old_z.astype(jnp.float32), precision=lax.Precision.HIGHEST, preferred_element_type=jnp.float32) + cross
    lower = jnp.linalg.cholesky(total)
    new_z = jax.scipy.linalg.solve_triangular(lower, rhs, lower=True)
    return (lower.T, new_z)
```

```python
import jax
import jax.numpy as jnp
from jax import lax
from jax.sharding import PartitionSpec as P

TILE = 128
AXES = ("rows", "grp")


def contract(left, right, precision=None):
    return lax.dot_general(
        left,
        right,
        (((0,), (0,)), ((), ())),
        precision=precision,
        preferred_element_type=jnp.float32,
    )


def butterfly_sum(local, n_dev):
    idx = lax.axis_index(AXES)
    steps = n_dev.bit_length() - 1
    cur = local
    for k in range(steps):
        pairs = [(i, i ^ (1 << k)) for i in range(n_dev)]
        half = cur.shape[0] // 2
        bit = (idx >> k) & 1
        keep = lax.dynamic_slice_in_dim(cur, bit * half, half, 0)
        send = lax.dynamic_slice_in_dim(cur, (1 - bit) * half, half, 0)
        cur = keep + lax.ppermute(send, AXES, pairs)
    for k in reversed(range(steps)):
        pairs = [(i, i ^ (1 << k)) for i in range(n_dev)]
        half = cur.shape[0]
        bit = (idx >> k) & 1
        got = lax.ppermute(cur, AXES, pairs)
        both = jnp.zeros((2 * half,) + cur.shape[1:], cur.dtype)
        both = lax.dynamic_update_slice_in_dim(both, cur, bit * half, 0)
        cur = lax.dynamic_update_slice_in_dim(both, got, (1 - bit) * half, 0)
    return cur


def summed(local, n_dev):
    rows = local.shape[0]
    if n_dev & (n_dev - 1) == 0 and rows % n_dev == 0:
        return butterfly_sum(local, n_dev)
    return lax.psum(local, AXES)


def body(slab_x, slab_y, row_mask, live_tiles, old_r, old_z):
    rows_here, width = slab_x.shape
    n_grp = lax.axis_size("grp")
    n_dev = lax.axis_size("rows") * n_grp
    tile_ids = lax.broadcasted_iota(jnp.int32, (rows_here,), 0) // TILE
    live = (row_mask == 1) & (tile_ids < live_tiles[0])
    masked = jnp.where(live[:, None], slab_x, jnp.zeros_like(slab_x))
    gram = contract(masked, slab_x)
    cross = contract(masked, slab_y)
    share = old_r.shape[0] // n_grp
    start = lax.axis_index("grp") * share
    r_part = lax.dynamic_slice_in_dim(old_r, start, share, 0)
    z_part = lax.dynamic_slice_in_dim(old_z, start, share, 0)
    gram = gram + contract(r_part, r_part, lax.Precision.HIGHEST)
    cross = cross + contract(r_part, z_part, lax.Precision.HIGHEST)
    both = summed(jnp.concatenate([gram, cross], axis=1), n_dev)
    total = both[:, :width]
    rhs = both[:, width:]
    lower = jnp.linalg.cholesky(total)
    new_z = jax.scipy.linalg.solve_triangular(lower, rhs, lower=True)
    return (lower.T, new_z)


def solution(mesh):
    placed = (
        P(AXES, None),
        P(AXES, None),
        P(AXES),
        P(AXES),
        P("rows", None),
        P("rows", None),
    )
    return jax.shard_map(body, mesh=mesh, in_specs=placed, out_specs=(P(), P()), check_vma=False)
```

```python
import jax
import jax.numpy as jnp
from jax import lax
from jax.sharding import PartitionSpec as P

TILE = 128
AXES = ("rows", "grp")


def contract(left, right, precision=None):
    return lax.dot_general(
        left,
        right,
        (((0,), (0,)), ((), ())),
        precision=precision,
        preferred_element_type=jnp.float32,
    )


def butterfly_sum(local, n_dev):
    idx = lax.axis_index(AXES)
    steps = n_dev.bit_length() - 1
    cur = local
    for k in range(steps):
        pairs = [(i, i ^ (1 << k)) for i in range(n_dev)]
        half = cur.shape[0] // 2
        low = ((idx >> k) & 1) == 0
        lo, hi = cur[:half], cur[half:]
        keep = jnp.where(low, lo, hi)
        send = jnp.where(low, hi, lo)
        cur = keep + lax.ppermute(send, AXES, pairs)
    for k in reversed(range(steps)):
        pairs = [(i, i ^ (1 << k)) for i in range(n_dev)]
        low = ((idx >> k) & 1) == 0
        got = lax.ppermute(cur, AXES, pairs)
        cur = jnp.where(low, jnp.concatenate([cur, got]), jnp.concatenate([got, cur]))
    return cur


def summed(local, n_dev):
    rows = local.shape[0]
    if n_dev & (n_dev - 1) == 0 and rows % n_dev == 0:
        return butterfly_sum(local, n_dev)
    return lax.psum(local, AXES)


def body(slab_x, slab_y, row_mask, live_tiles, old_r, old_z):
    rows_here, width = slab_x.shape
    n_grp = lax.axis_size("grp")
    n_dev = lax.axis_size("rows") * n_grp
    tile_ids = lax.broadcasted_iota(jnp.int32, (rows_here,), 0) // TILE
    live = (row_mask == 1) & (tile_ids < live_tiles[0])
    masked = jnp.where(live[:, None], slab_x, jnp.zeros_like(slab_x))
    gram = contract(masked, slab_x)
    cross = contract(masked, slab_y)
    share = old_r.shape[0] // n_grp
    start = lax.axis_index("grp") * share
    r_part = lax.dynamic_slice_in_dim(old_r, start, share, 0)
    z_part = lax.dynamic_slice_in_dim(old_z, start, share, 0)
    gram = gram + contract(r_part, r_part, lax.Precision.HIGHEST)
    cross = cross + contract(r_part, z_part, lax.Precision.HIGHEST)
    both = summed(jnp.concatenate([gram, cross], axis=1), n_dev)
    total = both[:, :width]
    rhs = both[:, width:]
    return factor_and_solve(total, rhs)


def factor_and_solve(total, rhs, block=128):
    n = total.shape[0]
    trail = jnp.concatenate([total, rhs.T], axis=0)
    columns = []
    for s in range(0, n, block):
        diag = lax.linalg.cholesky(trail[:block, :block], symmetrize_input=False)
        diag = jnp.tril(diag)
        panel = lax.linalg.triangular_solve(
            diag, trail[block:, :block], left_side=False, lower=True, transpose_a=True
        )
        columns.append(jnp.concatenate([diag, panel], axis=0))
        if s + block < n:
            upper = panel[: n - s - block]
            trail = trail[block:, block:] - lax.dot_general(
                panel,
                upper,
                (((1,), (1,)), ((), ())),
                precision=lax.Precision.HIGHEST,
                preferred_element_type=jnp.float32,
            )
    lower = jnp.concatenate(
        [jnp.pad(col[: n - s], ((s, 0), (0, 0))) for s, col in zip(range(0, n, block), columns)],
        axis=1,
    )
    new_z_t = jnp.concatenate([col[n - s :] for s, col in zip(range(0, n, block), columns)], axis=1)
    return (lower.T, new_z_t.T)


def solution(mesh):
    placed = (
        P(AXES, None),
        P(AXES, None),
        P(AXES),
        P(AXES),
        P("rows", None),
        P("rows", None),
    )
    return jax.shard_map(body, mesh=mesh, in_specs=placed, out_specs=(P(), P()), check_vma=False)
```

```python
import jax
import jax.numpy as jnp
from jax import lax
from jax.sharding import PartitionSpec as P

TILE = 128
AXES = ("rows", "grp")


def contract(left, right, precision=None):
    return lax.dot_general(
        left,
        right,
        (((0,), (0,)), ((), ())),
        precision=precision,
        preferred_element_type=jnp.float32,
    )


def butterfly_sum(local, n_dev):
    idx = lax.axis_index(AXES)
    steps = n_dev.bit_length() - 1
    cur = local
    for k in range(steps):
        pairs = [(i, i ^ (1 << k)) for i in range(n_dev)]
        half = cur.shape[0] // 2
        low = ((idx >> k) & 1) == 0
        lo, hi = cur[:half], cur[half:]
        keep = jnp.where(low, lo, hi)
        send = jnp.where(low, hi, lo)
        cur = keep + lax.ppermute(send, AXES, pairs)
    for k in reversed(range(steps)):
        pairs = [(i, i ^ (1 << k)) for i in range(n_dev)]
        low = ((idx >> k) & 1) == 0
        got = lax.ppermute(cur, AXES, pairs)
        cur = jnp.where(low, jnp.concatenate([cur, got]), jnp.concatenate([got, cur]))
    return cur


def summed(local, n_dev):
    rows = local.shape[0]
    if n_dev & (n_dev - 1) == 0 and rows % n_dev == 0:
        return butterfly_sum(local, n_dev)
    return lax.psum(local, AXES)


def body(slab_x, slab_y, row_mask, live_tiles, old_r, old_z):
    rows_here, width = slab_x.shape
    n_grp = lax.axis_size("grp")
    n_dev = lax.axis_size("rows") * n_grp
    tile_ids = lax.broadcasted_iota(jnp.int32, (rows_here,), 0) // TILE
    live = (row_mask == 1) & (tile_ids < live_tiles[0])
    masked = jnp.where(live[:, None], slab_x, jnp.zeros_like(slab_x))
    gram = contract(masked, slab_x)
    cross = contract(masked, slab_y)
    share = old_r.shape[0] // n_grp
    start = lax.axis_index("grp") * share
    r_part = lax.dynamic_slice_in_dim(old_r, start, share, 0)
    z_part = lax.dynamic_slice_in_dim(old_z, start, share, 0)
    gram = gram + contract(r_part, r_part, lax.Precision.HIGHEST)
    cross = cross + contract(r_part, z_part, lax.Precision.HIGHEST)
    both = summed(jnp.concatenate([gram.T, cross.T], axis=0), n_dev)
    return factor_and_solve(both[:width].T, both[width:])


def factor_and_solve(total, rhs_t, block=128):
    n = total.shape[0]
    trail = jnp.concatenate([total, rhs_t], axis=0)
    columns = []
    for s in range(0, n, block):
        diag = lax.linalg.cholesky(trail[:block, :block], symmetrize_input=False)
        diag = jnp.tril(diag)
        panel = lax.linalg.triangular_solve(
            diag, trail[block:, :block], left_side=False, lower=True, transpose_a=True
        )
        columns.append(jnp.concatenate([diag, panel], axis=0))
        if s + block < n:
            upper = panel[: n - s - block]
            trail = trail[block:, block:] - lax.dot_general(
                panel,
                upper,
                (((1,), (1,)), ((), ())),
                precision=lax.Precision.HIGHEST,
                preferred_element_type=jnp.float32,
            )
    lower = jnp.concatenate(
        [jnp.pad(col[: n - s], ((s, 0), (0, 0))) for s, col in zip(range(0, n, block), columns)],
        axis=1,
    )
    new_z_t = jnp.concatenate([col[n - s :] for s, col in zip(range(0, n, block), columns)], axis=1)
    return (lower.T, new_z_t.T)


def solution(mesh):
    placed = (
        P(AXES, None),
        P(AXES, None),
        P(AXES),
        P(AXES),
        P("rows", None),
        P("rows", None),
    )
    return jax.shard_map(body, mesh=mesh, in_specs=placed, out_specs=(P(), P()), check_vma=False)
```

```python
import jax
import jax.numpy as jnp
from jax import lax
from jax.sharding import PartitionSpec as P

TILE = 128
AXES = ("rows", "grp")


def contract(left, right, precision=None):
    return lax.dot_general(
        left,
        right,
        (((0,), (0,)), ((), ())),
        precision=precision,
        preferred_element_type=jnp.float32,
    )


def digit_groups(n_dev):
    bits = n_dev.bit_length() - 1
    groups = [(0, 1)] if bits else []
    k = 1
    while k < bits:
        width = min(2, bits - k)
        groups.append((k, width))
        k += width
    return groups


def pick(pieces, digit):
    out = pieces[-1]
    for t in range(len(pieces) - 2, -1, -1):
        out = jnp.where(digit == t, pieces[t], out)
    return out


def exchange_sum(local, n_dev):
    idx = lax.axis_index(AXES)
    groups = digit_groups(n_dev)
    cur = local
    for k, width in groups:
        radix = 1 << width
        digit = (idx >> k) & (radix - 1)
        size = cur.shape[0] // radix
        parts = [cur[t * size : (t + 1) * size] for t in range(radix)]
        acc = pick(parts, digit)
        for a in range(1, radix):
            pairs = [(i, i ^ (a << k)) for i in range(n_dev)]
            acc = acc + lax.ppermute(pick(parts, digit ^ a), AXES, pairs)
        cur = acc
    for k, width in reversed(groups):
        radix = 1 << width
        digit = (idx >> k) & (radix - 1)
        got = [cur]
        for a in range(1, radix):
            pairs = [(i, i ^ (a << k)) for i in range(n_dev)]
            got.append(lax.ppermute(cur, AXES, pairs))
        cur = jnp.concatenate([pick(got, digit ^ t) for t in range(radix)], axis=0)
    return cur


def summed(local, n_dev):
    rows = local.shape[0]
    if n_dev & (n_dev - 1) == 0 and rows % n_dev == 0 and n_dev > 1:
        return exchange_sum(local, n_dev)
    return lax.psum(local, AXES)


def body(slab_x, slab_y, row_mask, live_tiles, old_r, old_z):
    rows_here, width = slab_x.shape
    n_grp = lax.axis_size("grp")
    n_dev = lax.axis_size("rows") * n_grp
    tile_ids = lax.broadcasted_iota(jnp.int32, (rows_here,), 0) // TILE
    live = (row_mask == 1) & (tile_ids < live_tiles[0])
    masked = jnp.where(live[:, None], slab_x, jnp.zeros_like(slab_x))
    gram = contract(masked, slab_x)
    cross = contract(masked, slab_y)
    share = old_r.shape[0] // n_grp
    start = lax.axis_index("grp") * share
    r_part = lax.dynamic_slice_in_dim(old_r, start, share, 0)
    z_part = lax.dynamic_slice_in_dim(old_z, start, share, 0)
    gram = gram + contract(r_part, r_part, lax.Precision.HIGHEST)
    cross = cross + contract(r_part, z_part, lax.Precision.HIGHEST)
    both = summed(jnp.concatenate([gram.T, cross.T], axis=0), n_dev)
    return factor_and_solve(both[:width].T, both[width:])


def factor_and_solve(total, rhs_t, block=128):
    n = total.shape[0]
    trail = jnp.concatenate([total, rhs_t], axis=0)
    columns = []
    for s in range(0, n, block):
        diag = lax.linalg.cholesky(trail[:block, :block], symmetrize_input=False)
        panel = lax.linalg.triangular_solve(
            diag, trail[block:, :block], left_side=False, lower=True, transpose_a=True
        )
        columns.append(jnp.concatenate([diag, panel], axis=0))
        if s + block < n:
            upper = panel[: n - s - block]
            trail = trail[block:, block:] - lax.dot_general(
                panel,
                upper,
                (((1,), (1,)), ((), ())),
                precision=lax.Precision.HIGHEST,
                preferred_element_type=jnp.float32,
            )
    lower = jnp.concatenate(
        [jnp.pad(col[: n - s], ((s, 0), (0, 0))) for s, col in zip(range(0, n, block), columns)],
        axis=1,
    )
    new_z_t = jnp.concatenate([col[n - s :] for s, col in zip(range(0, n, block), columns)], axis=1)
    return (lower.T, new_z_t.T)


def solution(mesh):
    placed = (
        P(AXES, None),
        P(AXES, None),
        P(AXES),
        P(AXES),
        P("rows", None),
        P("rows", None),
    )
    return jax.shard_map(body, mesh=mesh, in_specs=placed, out_specs=(P(), P()), check_vma=False)
```

```python
import jax
import jax.numpy as jnp
from jax import lax
from jax.sharding import PartitionSpec as P

TILE = 128
AXES = ("rows", "grp")


def contract(left, right, precision=None):
    return lax.dot_general(
        left,
        right,
        (((0,), (0,)), ((), ())),
        precision=precision,
        preferred_element_type=jnp.float32,
    )


def digit_groups(n_dev):
    bits = n_dev.bit_length() - 1
    groups = [(0, 1)] if bits else []
    k = 1
    while k < bits:
        width = min(2, bits - k)
        groups.append((k, width))
        k += width
    return groups


def pick(pieces, digit):
    out = pieces[-1]
    for t in range(len(pieces) - 2, -1, -1):
        out = jnp.where(digit == t, pieces[t], out)
    return out


def exchange_sum(local, n_dev):
    idx = lax.axis_index(AXES)
    groups = digit_groups(n_dev)
    cur = local
    for k, width in groups:
        radix = 1 << width
        digit = (idx >> k) & (radix - 1)
        size = cur.shape[0] // radix
        parts = [cur[t * size : (t + 1) * size] for t in range(radix)]
        acc = pick(parts, digit)
        for a in range(1, radix):
            pairs = [(i, i ^ (a << k)) for i in range(n_dev)]
            acc = acc + lax.ppermute(pick(parts, digit ^ a), AXES, pairs)
        cur = acc
    for k, width in reversed(groups):
        radix = 1 << width
        digit = (idx >> k) & (radix - 1)
        got = [cur]
        for a in range(1, radix):
            pairs = [(i, i ^ (a << k)) for i in range(n_dev)]
            got.append(lax.ppermute(cur, AXES, pairs))
        cur = jnp.concatenate([pick(got, digit ^ t) for t in range(radix)], axis=0)
    return cur


def summed(local, n_dev):
    rows = local.shape[0]
    if n_dev & (n_dev - 1) == 0 and rows % n_dev == 0 and n_dev > 1:
        return exchange_sum(local, n_dev)
    return lax.psum(local, AXES)


def body(slab_x, slab_y, row_mask, live_tiles, old_r, old_z):
    rows_here, width = slab_x.shape
    n_grp = lax.axis_size("grp")
    n_dev = lax.axis_size("rows") * n_grp
    tile_ids = lax.broadcasted_iota(jnp.int32, (rows_here,), 0) // TILE
    live = (row_mask == 1) & (tile_ids < live_tiles[0])
    masked = jnp.where(live[:, None], slab_x, jnp.zeros_like(slab_x))
    gram = contract(masked, slab_x)
    cross = contract(masked, slab_y)
    share = old_r.shape[0] // n_grp
    start = lax.axis_index("grp") * share
    r_part = lax.dynamic_slice_in_dim(old_r, start, share, 0)
    z_part = lax.dynamic_slice_in_dim(old_z, start, share, 0)
    gram = gram + contract(r_part, r_part, lax.Precision.HIGHEST)
    cross = cross + contract(r_part, z_part, lax.Precision.HIGHEST)
    both = summed(jnp.concatenate([gram.T, cross.T], axis=0), n_dev)
    return factor_and_solve(both[:width].T, both[width:])


def factor_and_solve(total, rhs_t, block=128):
    n = total.shape[0]
    trail = jnp.concatenate([total, rhs_t], axis=0)
    rows = lax.broadcasted_iota(jnp.int32, (trail.shape[0], 1), 0)

    def step(b, carry):
        trail, out = carry
        s = b * block
        diag = lax.dynamic_slice(trail, (s, s), (block, block))
        diag = lax.linalg.cholesky(diag, symmetrize_input=False)
        col = lax.dynamic_slice_in_dim(trail, s, block, axis=1)
        panel = lax.linalg.triangular_solve(
            diag, col, left_side=False, lower=True, transpose_a=True
        )
        below = jnp.where(rows >= s + block, panel, 0.0)
        out = lax.dynamic_update_slice(out, lax.dynamic_update_slice(below, diag, (s, 0)), (0, s))
        trail = trail - lax.dot_general(
            below,
            below[:n],
            (((1,), (1,)), ((), ())),
            precision=lax.Precision.HIGHEST,
            preferred_element_type=jnp.float32,
        )
        return trail, out

    _, out = lax.fori_loop(0, n // block, step, (trail, jnp.zeros_like(trail)))
    return (out[:n].T, out[n:].T)


def solution(mesh):
    placed = (
        P(AXES, None),
        P(AXES, None),
        P(AXES),
        P(AXES),
        P("rows", None),
        P("rows", None),
    )
    return jax.shard_map(body, mesh=mesh, in_specs=placed, out_specs=(P(), P()), check_vma=False)
```

```python
import jax
import jax.numpy as jnp
from jax import lax
from jax.sharding import PartitionSpec as P

TILE = 128
AXES = ("rows", "grp")


def contract(left, right, precision=None):
    return lax.dot_general(
        left,
        right,
        (((0,), (0,)), ((), ())),
        precision=precision,
        preferred_element_type=jnp.float32,
    )


def digit_groups(n_dev):
    bits = n_dev.bit_length() - 1
    groups = [(0, 1)] if bits else []
    k = 1
    while k < bits:
        width = min(2, bits - k)
        groups.append((k, width))
        k += width
    return groups


def pick(pieces, digit):
    out = pieces[-1]
    for t in range(len(pieces) - 2, -1, -1):
        out = jnp.where(digit == t, pieces[t], out)
    return out


def exchange_sum(local, n_dev):
    idx = lax.axis_index(AXES)
    groups = digit_groups(n_dev)
    cur = local
    for k, width in groups:
        radix = 1 << width
        digit = (idx >> k) & (radix - 1)
        size = cur.shape[0] // radix
        parts = [cur[t * size : (t + 1) * size] for t in range(radix)]
        acc = pick(parts, digit)
        for a in range(1, radix):
            pairs = [(i, i ^ (a << k)) for i in range(n_dev)]
            acc = acc + lax.ppermute(pick(parts, digit ^ a), AXES, pairs)
        cur = acc
    for k, width in reversed(groups):
        radix = 1 << width
        digit = (idx >> k) & (radix - 1)
        got = [cur]
        for a in range(1, radix):
            pairs = [(i, i ^ (a << k)) for i in range(n_dev)]
            got.append(lax.ppermute(cur, AXES, pairs))
        cur = jnp.concatenate([pick(got, digit ^ t) for t in range(radix)], axis=0)
    return cur


def summed(local, n_dev):
    rows = local.shape[0]
    if n_dev & (n_dev - 1) == 0 and rows % n_dev == 0 and n_dev > 1:
        return exchange_sum(local, n_dev)
    return lax.psum(local, AXES)


def top_bits(v):
    t = v * 65537.0
    return t - (t - v)


def split3(v):
    hi = top_bits(v)
    rest = v - hi
    mid = top_bits(rest)
    lo = rest - mid
    return hi.astype(jnp.bfloat16), mid.astype(jnp.bfloat16), lo.astype(jnp.bfloat16)


def fine_product(left, right, axis):
    lh, lm, ll = split3(left)
    rh, rm, rl = split3(right)
    lefts = jnp.concatenate([lh, lh, lm, lh, lm, ll], axis=axis)
    rights = jnp.concatenate([rh, rm, rh, rl, rm, rh], axis=axis)
    return lax.dot_general(
        lefts, rights, (((axis,), (axis,)), ((), ())), preferred_element_type=jnp.float32
    )


def body(slab_x, slab_y, row_mask, live_tiles, old_r, old_z):
    rows_here, width = slab_x.shape
    n_grp = lax.axis_size("grp")
    n_dev = lax.axis_size("rows") * n_grp
    tile_ids = lax.broadcasted_iota(jnp.int32, (rows_here,), 0) // TILE
    live = (row_mask == 1) & (tile_ids < live_tiles[0])
    masked = jnp.where(live[:, None], slab_x, jnp.zeros_like(slab_x))
    gram = contract(masked, slab_x)
    cross = contract(masked, slab_y)
    share = old_r.shape[0] // n_grp
    start = lax.axis_index("grp") * share
    r_part = lax.dynamic_slice_in_dim(old_r, start, share, 0)
    z_part = lax.dynamic_slice_in_dim(old_z, start, share, 0)
    old = fine_product(r_part, jnp.concatenate([r_part, z_part], axis=1), 0)
    gram = gram + old[:, :width]
    cross = cross + old[:, width:]
    both = summed(jnp.concatenate([gram.T, cross.T], axis=0), n_dev)
    return factor_and_solve(both)


def factor_and_solve(trail, block=128):
    n = trail.shape[1]
    columns = []
    for s in range(0, n, block):
        diag = lax.linalg.cholesky(trail[:block, :block], symmetrize_input=False)
        panel = lax.linalg.triangular_solve(
            diag, trail[block:, :block], left_side=False, lower=True, transpose_a=True
        )
        columns.append(jnp.concatenate([diag, panel], axis=0))
        if s + block < n:
            upper = panel[: n - s - block]
            trail = trail[block:, block:] - lax.dot_general(
                panel,
                upper,
                (((1,), (1,)), ((), ())),
                precision=lax.Precision.HIGHEST,
                preferred_element_type=jnp.float32,
            )
    lower = jnp.concatenate(
        [jnp.pad(col[: n - s], ((s, 0), (0, 0))) for s, col in zip(range(0, n, block), columns)],
        axis=1,
    )
    new_z_t = jnp.concatenate([col[n - s :] for s, col in zip(range(0, n, block), columns)], axis=1)
    return (lower.T, new_z_t.T)


def solution(mesh):
    placed = (
        P(AXES, None),
        P(AXES, None),
        P(AXES),
        P(AXES),
        P("rows", None),
        P("rows", None),
    )
    return jax.shard_map(body, mesh=mesh, in_specs=placed, out_specs=(P(), P()), check_vma=False)
```

```python
import jax
import jax.numpy as jnp
from jax import lax
from jax.sharding import PartitionSpec as P

TILE = 128
AXES = ("rows", "grp")


def contract(left, right, precision=None):
    return lax.dot_general(
        left,
        right,
        (((0,), (0,)), ((), ())),
        precision=precision,
        preferred_element_type=jnp.float32,
    )


def digit_groups(n_dev):
    bits = n_dev.bit_length() - 1
    groups = [(0, 1)] if bits else []
    k = 1
    while k < bits:
        width = min(2, bits - k)
        groups.append((k, width))
        k += width
    return groups


def pick(pieces, digit):
    out = pieces[-1]
    for t in range(len(pieces) - 2, -1, -1):
        out = jnp.where(digit == t, pieces[t], out)
    return out


def exchange_sum(local, n_dev):
    idx = lax.axis_index(AXES)
    groups = digit_groups(n_dev)
    cur = local
    for k, width in groups:
        radix = 1 << width
        digit = (idx >> k) & (radix - 1)
        size = cur.shape[0] // radix
        parts = [cur[t * size : (t + 1) * size] for t in range(radix)]
        acc = pick(parts, digit)
        for a in range(1, radix):
            pairs = [(i, i ^ (a << k)) for i in range(n_dev)]
            acc = acc + lax.ppermute(pick(parts, digit ^ a), AXES, pairs)
        cur = acc
    for k, width in reversed(groups):
        radix = 1 << width
        digit = (idx >> k) & (radix - 1)
        got = [cur]
        for a in range(1, radix):
            pairs = [(i, i ^ (a << k)) for i in range(n_dev)]
            got.append(lax.ppermute(cur, AXES, pairs))
        cur = jnp.concatenate([pick(got, digit ^ t) for t in range(radix)], axis=0)
    return cur


def summed(local, n_dev):
    rows = local.shape[0]
    if n_dev & (n_dev - 1) == 0 and rows % n_dev == 0 and n_dev > 1:
        return exchange_sum(local, n_dev)
    return lax.psum(local, AXES)


def top_bits(v):
    t = v * 65537.0
    return t - (t - v)


def split3(v):
    hi = top_bits(v)
    rest = v - hi
    mid = top_bits(rest)
    lo = rest - mid
    return hi.astype(jnp.bfloat16), mid.astype(jnp.bfloat16), lo.astype(jnp.bfloat16)


def fine_product(left, right, axis):
    lh, lm, ll = split3(left)
    rh, rm, rl = split3(right)
    lefts = jnp.concatenate([lh, lh, lm, lh, lm, ll], axis=axis)
    rights = jnp.concatenate([rh, rm, rh, rl, rm, rh], axis=axis)
    return lax.dot_general(
        lefts, rights, (((axis,), (axis,)), ((), ())), preferred_element_type=jnp.float32
    )


def body(slab_x, slab_y, row_mask, live_tiles, old_r, old_z):
    rows_here, width = slab_x.shape
    n_grp = lax.axis_size("grp")
    n_dev = lax.axis_size("rows") * n_grp
    tile_ids = lax.broadcasted_iota(jnp.int32, (rows_here,), 0) // TILE
    live = (row_mask == 1) & (tile_ids < live_tiles[0])
    masked = jnp.where(live[:, None], slab_x, jnp.zeros_like(slab_x))
    gram = contract(masked, slab_x)
    cross = contract(masked, slab_y)
    share = old_r.shape[0] // n_grp
    start = lax.axis_index("grp") * share
    r_part = lax.dynamic_slice_in_dim(old_r, start, share, 0)
    z_part = lax.dynamic_slice_in_dim(old_z, start, share, 0)
    old = fine_product(r_part, jnp.concatenate([r_part, z_part], axis=1), 0)
    gram = gram + old[:, :width]
    cross = cross + old[:, width:]
    both = summed(jnp.concatenate([gram.T, cross.T], axis=0), n_dev)
    return factor_and_solve(both)


def factor_and_solve(trail, block=128):
    n = trail.shape[1]
    columns = []
    for s in range(0, n, block):
        diag = lax.linalg.cholesky_p.bind(trail[:block, :block])
        panel = lax.linalg.triangular_solve(
            diag, trail[block:, :block], left_side=False, lower=True, transpose_a=True
        )
        columns.append(jnp.concatenate([jnp.tril(diag), panel], axis=0))
        if s + block < n:
            upper = panel[: n - s - block]
            trail = trail[block:, block:] - lax.dot_general(
                panel,
                upper,
                (((1,), (1,)), ((), ())),
                precision=lax.Precision.HIGHEST,
                preferred_element_type=jnp.float32,
            )
    lower = jnp.concatenate(
        [jnp.pad(col[: n - s], ((s, 0), (0, 0))) for s, col in zip(range(0, n, block), columns)],
        axis=1,
    )
    new_z_t = jnp.concatenate([col[n - s :] for s, col in zip(range(0, n, block), columns)], axis=1)
    return (lower.T, new_z_t.T)


def solution(mesh):
    placed = (
        P(AXES, None),
        P(AXES, None),
        P(AXES),
        P(AXES),
        P("rows", None),
        P("rows", None),
    )
    return jax.shard_map(body, mesh=mesh, in_specs=placed, out_specs=(P(), P()), check_vma=False)
```

```python
import jax
import jax.numpy as jnp
from jax import lax
from jax.sharding import PartitionSpec as P

TILE = 128
AXES = ("rows", "grp")


def contract(left, right, precision=None):
    return lax.dot_general(
        left,
        right,
        (((0,), (0,)), ((), ())),
        precision=precision,
        preferred_element_type=jnp.float32,
    )


def digit_groups(n_dev):
    bits = n_dev.bit_length() - 1
    groups = [(0, 1)] if bits else []
    k = 1
    while k < bits:
        width = min(2, bits - k)
        groups.append((k, width))
        k += width
    return groups


def pick(pieces, digit):
    out = pieces[-1]
    for t in range(len(pieces) - 2, -1, -1):
        out = jnp.where(digit == t, pieces[t], out)
    return out


def exchange_sum(local, n_dev):
    idx = lax.axis_index(AXES)
    groups = digit_groups(n_dev)
    cur = local
    for k, width in groups:
        radix = 1 << width
        digit = (idx >> k) & (radix - 1)
        size = cur.shape[0] // radix
        acc = lax.dynamic_slice_in_dim(cur, digit * size, size, 0)
        for a in range(1, radix):
            pairs = [(i, i ^ (a << k)) for i in range(n_dev)]
            sent = lax.dynamic_slice_in_dim(cur, (digit ^ a) * size, size, 0)
            acc = acc + lax.ppermute(sent, AXES, pairs)
        cur = acc
    for k, width in reversed(groups):
        radix = 1 << width
        digit = (idx >> k) & (radix - 1)
        got = [cur]
        for a in range(1, radix):
            pairs = [(i, i ^ (a << k)) for i in range(n_dev)]
            got.append(lax.ppermute(cur, AXES, pairs))
        cur = jnp.concatenate([pick(got, digit ^ t) for t in range(radix)], axis=0)
    return cur


def summed(local, n_dev):
    rows = local.shape[0]
    if n_dev & (n_dev - 1) == 0 and rows % n_dev == 0 and n_dev > 1:
        return exchange_sum(local, n_dev)
    return lax.psum(local, AXES)


def top_bits(v):
    t = v * 65537.0
    return t - (t - v)


def split3(v):
    hi = top_bits(v)
    rest = v - hi
    mid = top_bits(rest)
    lo = rest - mid
    return hi.astype(jnp.bfloat16), mid.astype(jnp.bfloat16), lo.astype(jnp.bfloat16)


def fine_product(left, right, axis):
    lh, lm, ll = split3(left)
    rh, rm, rl = split3(right)
    lefts = jnp.concatenate([lh, lh, lm, lh, lm, ll], axis=axis)
    rights = jnp.concatenate([rh, rm, rh, rl, rm, rh], axis=axis)
    return lax.dot_general(
        lefts, rights, (((axis,), (axis,)), ((), ())), preferred_element_type=jnp.float32
    )


def body(slab_x, slab_y, row_mask, live_tiles, old_r, old_z):
    rows_here, width = slab_x.shape
    n_grp = lax.axis_size("grp")
    n_dev = lax.axis_size("rows") * n_grp
    tile_ids = lax.broadcasted_iota(jnp.int32, (rows_here,), 0) // TILE
    live = (row_mask == 1) & (tile_ids < live_tiles[0])
    masked = jnp.where(live[:, None], slab_x, jnp.zeros_like(slab_x))
    gram = contract(masked, slab_x)
    cross = contract(masked, slab_y)
    share = old_r.shape[0] // n_grp
    start = lax.axis_index("grp") * share
    r_part = lax.dynamic_slice_in_dim(old_r, start, share, 0)
    z_part = lax.dynamic_slice_in_dim(old_z, start, share, 0)
    old = fine_product(r_part, jnp.concatenate([r_part, z_part], axis=1), 0)
    gram = gram + old[:, :width]
    cross = cross + old[:, width:]
    both = summed(jnp.concatenate([gram.T, cross.T], axis=0), n_dev)
    return factor_and_solve(both)


def factor_and_solve(trail, block=128):
    n = trail.shape[1]
    columns = []
    for s in range(0, n, block):
        diag = lax.linalg.cholesky(trail[:block, :block], symmetrize_input=False)
        panel = lax.linalg.triangular_solve(
            diag, trail[block:, :block], left_side=False, lower=True, transpose_a=True
        )
        columns.append(jnp.concatenate([diag, panel], axis=0))
        if s + block < n:
            upper = panel[: n - s - block]
            trail = trail[block:, block:] - lax.dot_general(
                panel,
                upper,
                (((1,), (1,)), ((), ())),
                precision=lax.Precision.HIGHEST,
                preferred_element_type=jnp.float32,
            )
    lower = jnp.concatenate(
        [jnp.pad(col[: n - s], ((s, 0), (0, 0))) for s, col in zip(range(0, n, block), columns)],
        axis=1,
    )
    new_z_t = jnp.concatenate([col[n - s :] for s, col in zip(range(0, n, block), columns)], axis=1)
    return (lower.T, new_z_t.T)


def solution(mesh):
    placed = (
        P(AXES, None),
        P(AXES, None),
        P(AXES),
        P(AXES),
        P("rows", None),
        P("rows", None),
    )
    return jax.shard_map(body, mesh=mesh, in_specs=placed, out_specs=(P(), P()), check_vma=False)
```

```python
import jax
import jax.numpy as jnp
from jax import lax
from jax.sharding import PartitionSpec as P

TILE = 128
AXES = ("rows", "grp")


def contract(left, right, precision=None):
    return lax.dot_general(
        left,
        right,
        (((0,), (0,)), ((), ())),
        precision=precision,
        preferred_element_type=jnp.float32,
    )


def digit_groups(n_dev):
    bits = n_dev.bit_length() - 1
    groups = [(0, 1)] if bits else []
    k = 1
    while k < bits:
        width = min(2, bits - k)
        groups.append((k, width))
        k += width
    return groups


def pick(pieces, digit):
    out = pieces[-1]
    for t in range(len(pieces) - 2, -1, -1):
        out = jnp.where(digit == t, pieces[t], out)
    return out


def exchange_sum(local, n_dev):
    idx = lax.axis_index(AXES)
    groups = digit_groups(n_dev)
    cur = local
    for k, width in groups:
        radix = 1 << width
        digit = (idx >> k) & (radix - 1)
        size = cur.shape[0] // radix
        parts = [cur[t * size : (t + 1) * size] for t in range(radix)]
        acc = pick(parts, digit)
        for a in range(1, radix):
            pairs = [(i, i ^ (a << k)) for i in range(n_dev)]
            acc = acc + lax.ppermute(pick(parts, digit ^ a), AXES, pairs)
        cur = acc
    for k, width in reversed(groups):
        radix = 1 << width
        digit = (idx >> k) & (radix - 1)
        got = [cur]
        for a in range(1, radix):
            pairs = [(i, i ^ (a << k)) for i in range(n_dev)]
            got.append(lax.ppermute(cur, AXES, pairs))
        cur = jnp.concatenate([pick(got, digit ^ t) for t in range(radix)], axis=0)
    return cur


def summed(local, n_dev):
    rows = local.shape[0]
    if n_dev & (n_dev - 1) == 0 and rows % n_dev == 0 and n_dev > 1:
        return exchange_sum(local, n_dev)
    return lax.psum(local, AXES)


def top_bits(v):
    t = v * 65537.0
    return t - (t - v)


def split3(v):
    hi = top_bits(v)
    rest = v - hi
    mid = top_bits(rest)
    lo = rest - mid
    return hi.astype(jnp.bfloat16), mid.astype(jnp.bfloat16), lo.astype(jnp.bfloat16)


def fine_product(left, right, axis):
    lh, lm, ll = split3(left)
    rh, rm, rl = split3(right)
    lefts = jnp.concatenate([lh, lh, lm, lh, lm, ll], axis=axis)
    rights = jnp.concatenate([rh, rm, rh, rl, rm, rh], axis=axis)
    return lax.dot_general(
        lefts, rights, (((axis,), (axis,)), ((), ())), preferred_element_type=jnp.float32
    )


def body(slab_x, slab_y, row_mask, live_tiles, old_r, old_z):
    rows_here, width = slab_x.shape
    n_grp = lax.axis_size("grp")
    n_dev = lax.axis_size("rows") * n_grp
    tile_ids = lax.broadcasted_iota(jnp.int32, (rows_here,), 0) // TILE
    live = (row_mask == 1) & (tile_ids < live_tiles[0])
    masked = jnp.where(live[:, None], slab_x, jnp.zeros_like(slab_x))
    gram = contract(masked, slab_x)
    cross = contract(masked, slab_y)
    share = old_r.shape[0] // n_grp
    start = lax.axis_index("grp") * share
    r_part = lax.dynamic_slice_in_dim(old_r, start, share, 0)
    z_part = lax.dynamic_slice_in_dim(old_z, start, share, 0)
    old = fine_product(r_part, jnp.concatenate([r_part, z_part], axis=1), 0)
    gram = gram + old[:, :width]
    cross = cross + old[:, width:]
    both = summed(jnp.concatenate([gram.T, cross.T], axis=0), n_dev)
    return factor_and_solve(both)


def factor_and_solve(trail, block=128):
    n = trail.shape[1]
    columns = []
    for s in range(0, n, block):
        diag = lax.linalg.cholesky_p.bind(trail[:block, :block])
        panel = lax.linalg.triangular_solve(
            diag, trail[block:, :block], left_side=False, lower=True, transpose_a=True
        )
        columns.append(jnp.concatenate([diag, panel], axis=0))
        if s + block < n:
            upper = panel[: n - s - block]
            trail = trail[block:, block:] - lax.dot_general(
                panel,
                upper,
                (((1,), (1,)), ((), ())),
                precision=lax.Precision.HIGHEST,
                preferred_element_type=jnp.float32,
            )
    lower = jnp.tril(
        jnp.concatenate(
            [jnp.pad(col[: n - s], ((s, 0), (0, 0))) for s, col in zip(range(0, n, block), columns)],
            axis=1,
        )
    )
    new_z_t = jnp.concatenate([col[n - s :] for s, col in zip(range(0, n, block), columns)], axis=1)
    return (lower.T, new_z_t.T)


def solution(mesh):
    placed = (
        P(AXES, None),
        P(AXES, None),
        P(AXES),
        P(AXES),
        P("rows", None),
        P("rows", None),
    )
    return jax.shard_map(body, mesh=mesh, in_specs=placed, out_specs=(P(), P()), check_vma=False)
```

```python
import jax
import jax.numpy as jnp
from jax import lax
from jax.sharding import PartitionSpec as P

TILE = 128
AXES = ("rows", "grp")


def contract(left, right, precision=None):
    return lax.dot_general(
        left,
        right,
        (((0,), (0,)), ((), ())),
        precision=precision,
        preferred_element_type=jnp.float32,
    )


def digit_groups(n_dev):
    bits = n_dev.bit_length() - 1
    groups = [(0, 1)] if bits else []
    k = 1
    while k < bits:
        width = min(2, bits - k)
        groups.append((k, width))
        k += width
    return groups


def pick(pieces, digit):
    out = pieces[-1]
    for t in range(len(pieces) - 2, -1, -1):
        out = jnp.where(digit == t, pieces[t], out)
    return out


def exchange_sum(local, n_dev):
    idx = lax.axis_index(AXES)
    groups = digit_groups(n_dev)
    cur = local
    for k, width in groups:
        radix = 1 << width
        digit = (idx >> k) & (radix - 1)
        size = cur.shape[0] // radix
        parts = [cur[t * size : (t + 1) * size] for t in range(radix)]
        acc = pick(parts, digit)
        for a in range(1, radix):
            pairs = [(i, i ^ (a << k)) for i in range(n_dev)]
            acc = acc + lax.ppermute(pick(parts, digit ^ a), AXES, pairs)
        cur = acc
    for k, width in reversed(groups):
        radix = 1 << width
        digit = (idx >> k) & (radix - 1)
        got = [cur]
        for a in range(1, radix):
            pairs = [(i, i ^ (a << k)) for i in range(n_dev)]
            got.append(lax.ppermute(cur, AXES, pairs))
        cur = jnp.concatenate([pick(got, digit ^ t) for t in range(radix)], axis=0)
    return cur


def summed(local, n_dev):
    rows = local.shape[0]
    if n_dev & (n_dev - 1) == 0 and rows % n_dev == 0 and n_dev > 1:
        return exchange_sum(local, n_dev)
    return lax.psum(local, AXES)


def top_bits(v):
    t = v * 65537.0
    return t - (t - v)


def split3(v):
    hi = top_bits(v)
    rest = v - hi
    mid = top_bits(rest)
    lo = rest - mid
    return hi.astype(jnp.bfloat16), mid.astype(jnp.bfloat16), lo.astype(jnp.bfloat16)


def fine_product(left, right, axis):
    lh, lm, ll = split3(left)
    rh, rm, rl = split3(right)
    lefts = jnp.concatenate([lh, lh, lm, lh, lm, ll], axis=axis)
    rights = jnp.concatenate([rh, rm, rh, rl, rm, rh], axis=axis)
    return lax.dot_general(
        lefts, rights, (((axis,), (axis,)), ((), ())), preferred_element_type=jnp.float32
    )


def body(slab_x, slab_y, row_mask, live_tiles, old_r, old_z):
    rows_here, width = slab_x.shape
    n_grp = lax.axis_size("grp")
    n_dev = lax.axis_size("rows") * n_grp
    tile_ids = lax.broadcasted_iota(jnp.int32, (rows_here,), 0) // TILE
    live = (row_mask == 1) & (tile_ids < live_tiles[0])
    masked = jnp.where(live[:, None], slab_x, jnp.zeros_like(slab_x))
    gram = contract(masked, slab_x)
    cross = contract(masked, slab_y)
    share = old_r.shape[0] // n_grp
    start = lax.axis_index("grp") * share
    r_part = lax.dynamic_slice_in_dim(old_r, start, share, 0)
    z_part = lax.dynamic_slice_in_dim(old_z, start, share, 0)
    old = fine_product(r_part, jnp.concatenate([r_part, z_part], axis=1), 0)
    gram = gram + old[:, :width]
    cross = cross + old[:, width:]
    both = summed(jnp.concatenate([gram.T, cross.T], axis=0), n_dev)
    return factor_and_solve(both)


def factor_and_solve(trail, block=128):
    n = trail.shape[1]
    columns = []
    for s in range(0, n, block):
        diag = lax.linalg.cholesky(trail[:block, :block], symmetrize_input=False)
        panel = lax.linalg.triangular_solve(
            diag, trail[block:, :block], left_side=False, lower=True, transpose_a=True
        )
        columns.append(jnp.concatenate([diag, panel], axis=0))
        if s + block < n:
            upper = panel[: n - s - block]
            trail = trail[block:, block:] - lax.dot_general(
                panel,
                upper,
                (((1,), (1,)), ((), ())),
                precision=lax.Precision.HIGHEST,
                preferred_element_type=jnp.float32,
            )
    starts = range(0, n, block)
    new_r = jnp.concatenate(
        [jnp.pad(col[: n - s].T, ((0, 0), (s, 0))) for s, col in zip(starts, columns)], axis=0
    )
    new_z = jnp.concatenate([col[n - s :].T for s, col in zip(starts, columns)], axis=0)
    return (new_r, new_z)


def solution(mesh):
    placed = (
        P(AXES, None),
        P(AXES, None),
        P(AXES),
        P(AXES),
        P("rows", None),
        P("rows", None),
    )
    return jax.shard_map(body, mesh=mesh, in_specs=placed, out_specs=(P(), P()), check_vma=False)
```

```python
import jax
import jax.numpy as jnp
from jax import lax
from jax.sharding import PartitionSpec as P

TILE = 128
AXES = ("rows", "grp")


def contract(left, right, precision=None):
    return lax.dot_general(
        left,
        right,
        (((0,), (0,)), ((), ())),
        precision=precision,
        preferred_element_type=jnp.float32,
    )


def digit_groups(n_dev):
    bits = n_dev.bit_length() - 1
    groups = [(0, 1)] if bits else []
    k = 1
    while k < bits:
        width = min(2, bits - k)
        groups.append((k, width))
        k += width
    return groups


def pick(pieces, digit):
    out = pieces[-1]
    for t in range(len(pieces) - 2, -1, -1):
        out = jnp.where(digit == t, pieces[t], out)
    return out


def exchange_sum(local, n_dev):
    idx = lax.axis_index(AXES)
    groups = digit_groups(n_dev)
    cur = local
    for k, width in groups:
        radix = 1 << width
        digit = (idx >> k) & (radix - 1)
        size = cur.shape[0] // radix
        parts = [cur[t * size : (t + 1) * size] for t in range(radix)]
        acc = pick(parts, digit)
        for a in range(1, radix):
            pairs = [(i, i ^ (a << k)) for i in range(n_dev)]
            acc = acc + lax.ppermute(pick(parts, digit ^ a), AXES, pairs)
        cur = acc
    for k, width in reversed(groups):
        radix = 1 << width
        digit = (idx >> k) & (radix - 1)
        got = [cur]
        for a in range(1, radix):
            pairs = [(i, i ^ (a << k)) for i in range(n_dev)]
            got.append(lax.ppermute(cur, AXES, pairs))
        cur = jnp.concatenate([pick(got, digit ^ t) for t in range(radix)], axis=0)
    return cur


def summed(local, n_dev):
    rows = local.shape[0]
    if n_dev & (n_dev - 1) == 0 and rows % n_dev == 0 and n_dev > 1:
        return exchange_sum(local, n_dev)
    return lax.psum(local, AXES)


def top_bits(v):
    t = v * 65537.0
    return t - (t - v)


def split3(v):
    hi = top_bits(v)
    rest = v - hi
    mid = top_bits(rest)
    lo = rest - mid
    return hi.astype(jnp.bfloat16), mid.astype(jnp.bfloat16), lo.astype(jnp.bfloat16)


def fine_product(left, right, axis):
    lh, lm, ll = split3(left)
    rh, rm, rl = split3(right)
    lefts = jnp.concatenate([lh, lh, lm, lh, lm, ll], axis=axis)
    rights = jnp.concatenate([rh, rm, rh, rl, rm, rh], axis=axis)
    return lax.dot_general(
        lefts, rights, (((axis,), (axis,)), ((), ())), preferred_element_type=jnp.float32
    )


def body(slab_x, slab_y, row_mask, live_tiles, old_r, old_z):
    rows_here, width = slab_x.shape
    n_grp = lax.axis_size("grp")
    n_dev = lax.axis_size("rows") * n_grp
    tile_ids = lax.broadcasted_iota(jnp.int32, (rows_here,), 0) // TILE
    live = (row_mask == 1) & (tile_ids < live_tiles[0])
    masked = jnp.where(live[:, None], slab_x, jnp.zeros_like(slab_x))
    gram = contract(masked, slab_x)
    cross = contract(masked, slab_y)
    share = old_r.shape[0] // n_grp
    start = lax.axis_index("grp") * share
    r_part = lax.dynamic_slice_in_dim(old_r, start, share, 0)
    z_part = lax.dynamic_slice_in_dim(old_z, start, share, 0)
    old_t = fine_product(jnp.concatenate([r_part, z_part], axis=1), r_part, 0)
    both = summed(jnp.concatenate([gram.T, cross.T], axis=0) + old_t, n_dev)
    return factor_and_solve(both)


def factor_and_solve(trail, block=128):
    n = trail.shape[1]
    columns = []
    for s in range(0, n, block):
        diag = lax.linalg.cholesky(trail[:block, :block], symmetrize_input=False)
        panel = lax.linalg.triangular_solve(
            diag, trail[block:, :block], left_side=False, lower=True, transpose_a=True
        )
        columns.append(jnp.concatenate([diag, panel], axis=0))
        if s + block < n:
            upper = panel[: n - s - block]
            trail = trail[block:, block:] - lax.dot_general(
                panel,
                upper,
                (((1,), (1,)), ((), ())),
                precision=lax.Precision.HIGHEST,
                preferred_element_type=jnp.float32,
            )
    lower = jnp.concatenate(
        [jnp.pad(col[: n - s], ((s, 0), (0, 0))) for s, col in zip(range(0, n, block), columns)],
        axis=1,
    )
    new_z_t = jnp.concatenate([col[n - s :] for s, col in zip(range(0, n, block), columns)], axis=1)
    return (lower.T, new_z_t.T)


def solution(mesh):
    placed = (
        P(AXES, None),
        P(AXES, None),
        P(AXES),
        P(AXES),
        P("rows", None),
        P("rows", None),
    )
    return jax.shard_map(body, mesh=mesh, in_specs=placed, out_specs=(P(), P()), check_vma=False)
```

```python
import jax
import jax.numpy as jnp
from jax import lax
from jax.sharding import PartitionSpec as P

TILE = 128
AXES = ("rows", "grp")


def contract(left, right, precision=None):
    return lax.dot_general(
        left,
        right,
        (((0,), (0,)), ((), ())),
        precision=precision,
        preferred_element_type=jnp.float32,
    )


def digit_groups(n_dev):
    bits = n_dev.bit_length() - 1
    groups = [(0, 1)] if bits else []
    k = 1
    while k < bits:
        width = min(2, bits - k)
        groups.append((k, width))
        k += width
    return groups


def pick(pieces, digit):
    out = pieces[-1]
    for t in range(len(pieces) - 2, -1, -1):
        out = jnp.where(digit == t, pieces[t], out)
    return out


def exchange_sum(local, n_dev):
    idx = lax.axis_index(AXES)
    groups = digit_groups(n_dev)
    cur = local
    for k, width in groups:
        radix = 1 << width
        digit = (idx >> k) & (radix - 1)
        size = cur.shape[0] // radix
        parts = [cur[t * size : (t + 1) * size] for t in range(radix)]
        acc = pick(parts, digit)
        for a in sorted(range(1, radix), key=lambda a: (a != 2, a)):
            pairs = [(i, i ^ (a << k)) for i in range(n_dev)]
            acc = acc + lax.ppermute(pick(parts, digit ^ a), AXES, pairs)
        cur = acc
    for k, width in reversed(groups):
        radix = 1 << width
        digit = (idx >> k) & (radix - 1)
        got = {0: cur}
        for a in sorted(range(1, radix), key=lambda a: (a != 2, a)):
            pairs = [(i, i ^ (a << k)) for i in range(n_dev)]
            got[a] = lax.ppermute(cur, AXES, pairs)
        got = [got[a] for a in range(radix)]
        cur = jnp.concatenate([pick(got, digit ^ t) for t in range(radix)], axis=0)
    return cur


def summed(local, n_dev):
    rows = local.shape[0]
    if n_dev & (n_dev - 1) == 0 and rows % n_dev == 0 and n_dev > 1:
        return exchange_sum(local, n_dev)
    return lax.psum(local, AXES)


def top_bits(v):
    t = v * 65537.0
    return t - (t - v)


def split3(v):
    hi = top_bits(v)
    rest = v - hi
    mid = top_bits(rest)
    lo = rest - mid
    return hi.astype(jnp.bfloat16), mid.astype(jnp.bfloat16), lo.astype(jnp.bfloat16)


def fine_product(left, right, axis):
    lh, lm, ll = split3(left)
    rh, rm, rl = split3(right)
    lefts = jnp.concatenate([lh, lh, lm, lh, lm, ll], axis=axis)
    rights = jnp.concatenate([rh, rm, rh, rl, rm, rh], axis=axis)
    return lax.dot_general(
        lefts, rights, (((axis,), (axis,)), ((), ())), preferred_element_type=jnp.float32
    )


def body(slab_x, slab_y, row_mask, live_tiles, old_r, old_z):
    rows_here, width = slab_x.shape
    n_grp = lax.axis_size("grp")
    n_dev = lax.axis_size("rows") * n_grp
    tile_ids = lax.broadcasted_iota(jnp.int32, (rows_here,), 0) // TILE
    live = (row_mask == 1) & (tile_ids < live_tiles[0])
    masked = jnp.where(live[:, None], slab_x, jnp.zeros_like(slab_x))
    gram = contract(masked, slab_x)
    cross = contract(masked, slab_y)
    share = old_r.shape[0] // n_grp
    start = lax.axis_index("grp") * share
    r_part = lax.dynamic_slice_in_dim(old_r, start, share, 0)
    z_part = lax.dynamic_slice_in_dim(old_z, start, share, 0)
    old_t = fine_product(jnp.concatenate([r_part, z_part], axis=1), r_part, 0)
    both = summed(jnp.concatenate([gram.T, cross.T], axis=0) + old_t, n_dev)
    return factor_and_solve(both)


def factor_and_solve(trail, block=128):
    n = trail.shape[1]
    columns = []
    for s in range(0, n, block):
        diag = lax.linalg.cholesky(trail[:block, :block], symmetrize_input=False)
        panel = lax.linalg.triangular_solve(
            diag, trail[block:, :block], left_side=False, lower=True, transpose_a=True
        )
        columns.append(jnp.concatenate([diag, panel], axis=0))
        if s + block < n:
            upper = panel[: n - s - block]
            trail = trail[block:, block:] - lax.dot_general(
                panel,
                upper,
                (((1,), (1,)), ((), ())),
                precision=lax.Precision.HIGHEST,
                preferred_element_type=jnp.float32,
            )
    lower = jnp.concatenate(
        [jnp.pad(col[: n - s], ((s, 0), (0, 0))) for s, col in zip(range(0, n, block), columns)],
        axis=1,
    )
    new_z_t = jnp.concatenate([col[n - s :] for s, col in zip(range(0, n, block), columns)], axis=1)
    return (lower.T, new_z_t.T)


def solution(mesh):
    placed = (
        P(AXES, None),
        P(AXES, None),
        P(AXES),
        P(AXES),
        P("rows", None),
        P("rows", None),
    )
    return jax.shard_map(body, mesh=mesh, in_specs=placed, out_specs=(P(), P()), check_vma=False)
```
